256 devices in a mesh: dp: 32 (over x, z_hi, y), mp: 8 (over z_lo, core).
Axes of the slice: x: 4, y: 4, z: 8 (z_hi: 2, z_lo: 4; z = z_hi * 4 + z_lo), core: 2. Of those that a mesh axis runs over, the one named last changes fastest.
Arguments:
- store_rows: bfloat16 [8192, 8192], P('dp', 'mp'), may hold values from -6 to 6
- source_shard: int32 [1024], replicated, may hold values from 0 to 31, as said below
- source_row: int32 [1024], replicated, may hold values from 0 to 255
- state_len: int32 [32], replicated, may hold values from 1 to 64, 1024 in all
- visits: int32 [32], replicated, may hold values from 1 to 4095
- gain: bfloat16 [8192], P('mp'), may hold values from 0.5 to 1.5
- w_gate: bfloat16 [8192, 22016], P('mp', 'dp'), may hold values from -0.0625 to 0.0625
- w_up: bfloat16 [8192, 22016], P('mp', 'dp'), may hold values from -0.0625 to 0.0625
- w_down: bfloat16 [22016, 8192], P('dp', 'mp'), may hold values from -0.0390625 to 0.0390625
- upstream: bfloat16 [1024, 8192], P(None, 'mp'), may hold values from -0.375 to 0.375
Outputs:
- layer_out: bfloat16 [1024, 8192], P('dp', 'mp')
- grad_gate: bfloat16 [8192, 22016], P('mp', 'dp')
- grad_up: bfloat16 [8192, 22016], P('mp', 'dp')
- grad_down: bfloat16 [22016, 8192], P('dp', 'mp')
The draws below stay inside these ranges and needn't reach their ends.
Inputs may be any that keep to these rules, and one draw needn't show every extreme that they name: `source_shard`: block b holds training rows b * 32 to (b + 1) * 32 - 1. No shard is named more than 4 times in one block nor more than 128 times in all; one shard, drawn from the seed, is named exactly 4 times in every block. `state_len`: the lengths sum to 1024.
All inputs are finite; a program needn't handle non-finite values.
Results may differ from the reference program's by a relative error of at most 0.017.
Values may be sent and summed in bfloat16 or wider, within the bound.
No kernel may reach another device: no remote copies, remote signals or barrier semaphores. Data moves between devices by JAX's collectives and lax.ppermute only.
A program may use at most 64 MiB of HBM per device.

```python
import math
import jax
import jax.numpy as jnp
import numpy as np
from jax import lax

D = 8192
FF = 22016
ROW_DP = 32
STORE_DEV = 256
ROWS = 1024
STORE = 8192
STATES = 32
LEN_MAX = 64
PAIR_CAP = 4
N_DP = 32


def draw_source_shard(key, part):
    key_hot = jax.random.fold_in(key, 11)
    key_order = jax.random.fold_in(key, 12)
    key_place = jax.random.fold_in(key, 13)
    hot_shard = jax.random.randint(key_hot, (), 0, N_DP).astype(jnp.int32)
    others = ((hot_shard + 1 + jax.random.permutation(key_order, N_DP - 1).astype(jnp.int32)) % N_DP).astype(jnp.int32)
    homes = jnp.arange(N_DP, dtype=jnp.int32)
    place_keys = jax.vmap(lambda home: jax.random.fold_in(key_place, home))(homes)
    places = jax.vmap(lambda one_key: jax.random.permutation(one_key, ROW_DP))(place_keys).astype(jnp.int32)
    cold_count = ROW_DP - PAIR_CAP
    cold_slot = ((places - PAIR_CAP + homes[:, None] * cold_count) % (N_DP - 1)).astype(jnp.int32)
    source = jnp.where(places < PAIR_CAP, hot_shard, others[cold_slot])
    return source.reshape(-1).astype(jnp.int32)


def with_ends(drawn, rng, low, high):
    shape = drawn.shape
    index_at = [jax.random.randint(jax.random.fold_in(rng, axis), (), 0, shape[axis]) for axis in range(len(shape))]
    drawn = drawn.at[tuple(index_at)].set(low)
    longest = shape.index(max(shape))
    index_at[longest] = (index_at[longest] + 1) % shape[longest]
    return drawn.at[tuple(index_at)].set(high)


def steps_of(stream_key, dims, pieces, smallest, top_value):
    def one(dim, blocks):
        heights = jax.random.uniform(jax.random.fold_in(jax.random.fold_in(stream_key, 6), dim), (blocks,), jnp.float32, smallest / len(pieces), top_value / len(pieces))
        return jnp.repeat(jnp.exp(heights), dims[dim] // blocks).reshape((-1,) + (1,) * (len(dims) - dim - 1))

    factor_of = one(*pieces[0])
    for cut in pieces[1:]:
        factor_of = factor_of * one(*cut)
    return factor_of


def profile(amount, total, reach, lean):
    loads = [(1 << 20) // math.isqrt(grade ** lean) + 1 for grade in range(2, amount + 1)]
    spare, holding = total - reach - (amount - 1), [1] * (amount - 1)
    while spare > 0:
        movable = [i for i in range(amount - 1) if holding[i] < reach]
        mass, left = sum([loads[i] for i in movable]), spare
        for i in movable:
            more = min(reach - holding[i], max(1, left * loads[i] // mass), spare)
            holding[i] = holding[i] + more
            spare = spare - more
    return np.array([reach] + holding)


def uneven(own_key, amount, total, bound, slope):
    if amount == 2:
        one = jax.random.randint(own_key, (), max(1, total - bound), min(bound, total - 1) + 1)
        return jnp.stack([one, total - one])
    tallies = jnp.asarray(profile(amount, total, bound, slope), jnp.int32)
    pairs = (amount - 1) // 2
    donor, taker = tallies[1:1 + 2 * pairs:2], tallies[2:2 + 2 * pairs:2]
    room = jnp.minimum(donor - 1, bound - taker)
    passed = jax.random.randint(jax.random.fold_in(own_key, 1), (pairs,), 0, 1 << 20) % (room + 1)
    tallies = tallies.at[1:1 + 2 * pairs:2].set(donor - passed).at[2:2 + 2 * pairs:2].set(taker + passed)
    return tallies[jax.random.permutation(jax.random.fold_in(own_key, 2), amount)]


def centred(rng, dims, width, reach, pieces=(), held_as=jnp.bfloat16):
    entries = width * jax.random.normal(rng, dims, jnp.float32)
    if pieces:
        entries = entries * steps_of(rng, dims, pieces, -0.22, 0.18)
    return jnp.clip(entries, -reach, reach).astype(held_as)


def setup_inputs(seed: int = 0) -> dict:
    streams_of = jax.random.split(jax.random.key(seed), 11)
    return {
        "store_rows": centred(streams_of[0], (STORE, D), 1.0, 6.0, ((0, 32), (1, 8))),
        "source_shard": draw_source_shard(jax.random.fold_in(streams_of[10], 71), 0),
        "source_row": with_ends(jax.random.randint(streams_of[2], (ROWS,), 0, STORE_DEV), jax.random.fold_in(streams_of[2], 1), 0, STORE_DEV - 1).astype(jnp.int32),
        "state_len": uneven(streams_of[3], STATES, ROWS, LEN_MAX, 1).astype(jnp.int32),
        "visits": with_ends(jax.random.randint(streams_of[4], (STATES,), 1, 4096), jax.random.fold_in(streams_of[4], 1), 1, 4095).astype(jnp.int32),
        "gain": jnp.clip(1.0 + 0.1 * jax.random.normal(streams_of[5], (D,), jnp.float32), 0.5, 1.5).astype(jnp.bfloat16),
        "w_gate": centred(streams_of[6], (D, FF), D ** -0.5, 0.0625, ((0, 8), (1, 32))),
        "w_up": centred(streams_of[7], (D, FF), D ** -0.5, 0.0625, ((0, 8), (1, 32))),
        "w_down": centred(streams_of[8], (FF, D), FF ** -0.5, 0.0390625, ((0, 32), (1, 8))),
        "upstream": centred(streams_of[9], (ROWS, D), (2.0 / ROWS ** 0.5), 0.375, ((1, 8),)),
    }


epsilon = 1e-05

def reference(store_rows, source_shard, source_row, state_len, visits, gain, w_gate, w_up, w_down, upstream):
    index = (source_shard * STORE_DEV + source_row).astype(jnp.int32)
    train_rows = store_rows[index].astype(jnp.float32)
    squares = lax.optimization_barrier(jnp.sum(train_rows * train_rows, axis=1))
    inverse = lax.rsqrt(squares / D + epsilon)
    scaled = (train_rows * gain.astype(jnp.float32)[None, :]).astype(jnp.bfloat16)
    gate = inverse[:, None] * jnp.dot(scaled, w_gate, preferred_element_type=jnp.float32)
    up_all = inverse[:, None] * jnp.dot(scaled, w_up, preferred_element_type=jnp.float32)
    hidden = (jax.nn.silu(gate) * up_all).astype(jnp.bfloat16)
    layer_out = (train_rows + jnp.dot(hidden, w_down, preferred_element_type=jnp.float32)).astype(jnp.bfloat16)
    ends = jnp.cumsum(state_len).astype(jnp.int32)
    starts = (ends - state_len).astype(jnp.int32)
    row_ids = jnp.arange(ROWS, dtype=jnp.int32)
    member = ((row_ids[:, None] >= starts[None, :]) & (row_ids[:, None] < ends[None, :])).astype(jnp.float32)
    importance = jnp.log1p(visits.astype(jnp.float32))
    per_state = ROWS * importance / (state_len.astype(jnp.float32) * jnp.sum(importance))
    row_weight = lax.optimization_barrier(jnp.sum(member * per_state[None, :], axis=1))
    out_grad = (upstream.astype(jnp.float32) * row_weight[:, None]).astype(jnp.bfloat16)
    grad_down = jnp.dot(hidden.T, out_grad, preferred_element_type=jnp.float32).astype(jnp.bfloat16)
    grad_hidden = jnp.dot(out_grad, w_down.T, preferred_element_type=jnp.float32)
    sigmoid_gate = jax.nn.sigmoid(gate)
    gate_delta = (inverse[:, None] * grad_hidden * up_all * sigmoid_gate * (1.0 + gate * (1.0 - sigmoid_gate))).astype(jnp.bfloat16)
    up_delta = (inverse[:, None] * grad_hidden * gate * sigmoid_gate).astype(jnp.bfloat16)
    grad_gate = jnp.dot(scaled.T, gate_delta, preferred_element_type=jnp.float32).astype(jnp.bfloat16)
    grad_up = jnp.dot(scaled.T, up_delta, preferred_element_type=jnp.float32).astype(jnp.bfloat16)
    return (layer_out, grad_gate, grad_up, grad_down)
```

```python
import jax
import jax.numpy as jnp
from jax import lax
from jax.sharding import Mesh
from jax.sharding import PartitionSpec as P

D = 8192

epsilon = 1e-05

DP = ("x", "zh", "y")
MP = ("zl", "c")


def shards(
    store_rows, source_shard, source_row, state_len, visits, gain, w_gate, w_up, w_down, upstream
):
    f32, bf16 = jnp.float32, jnp.bfloat16
    count_dp = 1
    for name in DP:
        count_dp *= lax.axis_size(name)
    index_dp = lax.axis_index(DP)
    total_rows = source_shard.shape[0]
    block_rows = total_rows // count_dp
    pair_cap = max(block_rows // 8, 1)
    store_dev = store_rows.shape[0]
    hidden_dev = w_gate.shape[1]

    shard = source_shard.reshape(count_dp, block_rows)
    srow = source_row.reshape(count_dp, block_rows)
    same = shard[:, :, None] == shard[:, None, :]
    t_ids = jnp.arange(block_rows, dtype=jnp.int32)
    earlier = t_ids[None, :] < t_ids[:, None]
    rank = jnp.sum((same & earlier[None]).astype(jnp.int32), axis=2)

    owned = shard == index_dp
    slots = jnp.arange(pair_cap, dtype=jnp.int32)
    hit = owned[:, :, None] & (rank[:, :, None] == slots[None, None, :])
    slot_row = jnp.sum(jnp.where(hit, srow[:, :, None] + 1, 0), axis=1) - 1
    pick_out = (
        slot_row.reshape(count_dp * pair_cap)[:, None]
        == jnp.arange(store_dev, dtype=jnp.int32)[None, :]
    ).astype(bf16)
    outgoing = jnp.dot(pick_out, store_rows, preferred_element_type=f32).astype(bf16)
    received = lax.all_to_all(outgoing, DP, 0, 0, tiled=True)

    my_shard = lax.dynamic_index_in_dim(shard, index_dp, 0, keepdims=False)
    my_rank = lax.dynamic_index_in_dim(rank, index_dp, 0, keepdims=False)
    pick_in = (
        (my_shard * pair_cap + my_rank)[:, None]
        == jnp.arange(count_dp * pair_cap, dtype=jnp.int32)[None, :]
    ).astype(bf16)
    own_rows = jnp.dot(pick_in, received, preferred_element_type=f32).astype(bf16)

    train_rows = own_rows
    for name in reversed(DP):
        train_rows = lax.all_gather(train_rows, name, axis=0, tiled=True)

    rows_float = train_rows.astype(f32)
    squares = jnp.sum(rows_float * rows_float, axis=1)
    scaled = (rows_float * gain.astype(f32)[None, :]).astype(bf16)
    gate_term = jnp.dot(scaled, w_gate, preferred_element_type=f32)
    up_term = jnp.dot(scaled, w_up, preferred_element_type=f32)
    packed = jnp.concatenate([gate_term, up_term, squares[:, None]], axis=1)
    total = lax.psum(packed, MP)
    gate_total = total[:, :hidden_dev]
    up_total = total[:, hidden_dev : 2 * hidden_dev]
    square_total = total[:, 2 * hidden_dev]
    inverse = lax.rsqrt(square_total / D + epsilon)
    gate_all = inverse[:, None] * gate_total
    up_all = inverse[:, None] * up_total
    hidden_all = (jax.nn.silu(gate_all) * up_all).astype(bf16)

    down_part = jnp.dot(hidden_all, w_down, preferred_element_type=f32).astype(bf16)
    down_in = lax.all_to_all(down_part, DP, 0, 0, tiled=True)
    down_block = jnp.sum(
        down_in.reshape(count_dp, block_rows, down_in.shape[1]).astype(f32), axis=0
    )
    layer_out = (own_rows.astype(f32) + down_block).astype(bf16)

    row_ids = jnp.arange(total_rows, dtype=jnp.int32)
    ends = jnp.cumsum(state_len)
    starts = ends - state_len
    member = ((row_ids[:, None] >= starts[None, :]) & (row_ids[:, None] < ends[None, :])).astype(
        f32
    )
    importance = jnp.log1p(visits.astype(f32))
    per_state = total_rows * importance / (state_len.astype(f32) * jnp.sum(importance))
    row_weight = jnp.sum(member * per_state[None, :], axis=1)
    out_grad = (upstream.astype(f32) * row_weight[:, None]).astype(bf16)
    grad_down = lax.dot_general(
        hidden_all, out_grad, (((0,), (0,)), ((), ())), preferred_element_type=f32
    ).astype(bf16)
    hidden_term = lax.dot_general(
        out_grad, w_down, (((1,), (1,)), ((), ())), preferred_element_type=f32
    ).astype(bf16)
    grad_hidden = lax.psum(hidden_term, MP).astype(f32)
    sigmoid_gate = jax.nn.sigmoid(gate_all)
    gate_delta = (
        inverse[:, None]
        * grad_hidden
        * up_all
        * sigmoid_gate
        * (1.0 + gate_all * (1.0 - sigmoid_gate))
    ).astype(bf16)
    up_delta = (inverse[:, None] * grad_hidden * gate_all * sigmoid_gate).astype(bf16)
    grad_gate = lax.dot_general(
        scaled, gate_delta, (((0,), (0,)), ((), ())), preferred_element_type=f32
    ).astype(bf16)
    grad_up = lax.dot_general(
        scaled, up_delta, (((0,), (0,)), ((), ())), preferred_element_type=f32
    ).astype(bf16)
    return (layer_out, grad_gate, grad_up, grad_down)


def solution(mesh):
    sizes = dict(zip(mesh.axis_names, mesh.devices.shape))
    count_mp = sizes["mp"]
    count_dp = sizes["dp"]
    zh = 2
    y = 4
    x = count_dp // (zh * y)
    c = 2
    zl = count_mp // c
    view = Mesh(mesh.devices.reshape(x, zh, y, zl, c), DP + MP)
    in_specs = (
        P(DP, MP),
        P(),
        P(),
        P(),
        P(),
        P(MP),
        P(MP, DP),
        P(MP, DP),
        P(DP, MP),
        P(None, MP),
    )
    out_specs = (P(DP, MP), P(MP, DP), P(MP, DP), P(DP, MP))
    return jax.shard_map(shards, mesh=view, in_specs=in_specs, out_specs=out_specs, check_vma=False)
```

```python
import jax
import jax.numpy as jnp
from jax import lax
from jax.sharding import Mesh
from jax.sharding import PartitionSpec as P

D = 8192

epsilon = 1e-05

DP = ("x", "zh", "y")
MP = ("zl", "c")


def body(
    store_rows, source_shard, source_row, state_len, visits, gain, w_gate, w_up, w_down, upstream
):
    f32, bf16 = jnp.float32, jnp.bfloat16
    count_dp = 1
    for name in DP:
        count_dp *= lax.axis_size(name)
    index_dp = lax.axis_index(DP)
    total_rows = source_shard.shape[0]
    block_rows = total_rows // count_dp
    pair_cap = max(block_rows // 8, 1)
    store_dev = store_rows.shape[0]
    hidden_dev = w_gate.shape[1]

    shard = source_shard.reshape(count_dp, block_rows)
    srow = source_row.reshape(count_dp, block_rows)
    same = shard[:, :, None] == shard[:, None, :]
    t_ids = jnp.arange(block_rows, dtype=jnp.int32)
    earlier = t_ids[None, :] < t_ids[:, None]
    rank = jnp.sum((same & earlier[None]).astype(jnp.int32), axis=2)

    owned = shard == index_dp
    slots = jnp.arange(pair_cap, dtype=jnp.int32)
    hit = owned[:, :, None] & (rank[:, :, None] == slots[None, None, :])
    slot_row = jnp.sum(jnp.where(hit, srow[:, :, None] + 1, 0), axis=1) - 1
    pick_out = (
        slot_row.reshape(count_dp * pair_cap)[:, None]
        == jnp.arange(store_dev, dtype=jnp.int32)[None, :]
    ).astype(bf16)
    outgoing = jnp.dot(pick_out, store_rows, preferred_element_type=f32).astype(bf16)
    received = lax.all_to_all(outgoing, DP, 0, 0, tiled=True)

    my_shard = lax.dynamic_index_in_dim(shard, index_dp, 0, keepdims=False)
    my_rank = lax.dynamic_index_in_dim(rank, index_dp, 0, keepdims=False)
    pick_in = (
        (my_shard * pair_cap + my_rank)[:, None]
        == jnp.arange(count_dp * pair_cap, dtype=jnp.int32)[None, :]
    ).astype(bf16)
    own_rows = jnp.dot(pick_in, received, preferred_element_type=f32).astype(bf16)

    train_rows = own_rows
    for name in reversed(DP):
        train_rows = lax.all_gather(train_rows, name, axis=0, tiled=True)

    rows_float = train_rows.astype(f32)
    squares = jnp.sum(rows_float * rows_float, axis=1)
    scaled = (rows_float * gain.astype(f32)[None, :]).astype(bf16)
    gate_term = jnp.dot(scaled, w_gate, preferred_element_type=f32)
    up_term = jnp.dot(scaled, w_up, preferred_element_type=f32)
    packed = jnp.concatenate([gate_term, up_term, squares[:, None]], axis=1).astype(bf16)
    total = lax.psum(packed, MP).astype(f32)
    gate_total = total[:, :hidden_dev]
    up_total = total[:, hidden_dev : 2 * hidden_dev]
    square_total = total[:, 2 * hidden_dev]
    inverse = lax.rsqrt(square_total / D + epsilon)
    gate_all = inverse[:, None] * gate_total
    up_all = inverse[:, None] * up_total
    hidden_all = (jax.nn.silu(gate_all) * up_all).astype(bf16)

    down_part = jnp.dot(hidden_all, w_down, preferred_element_type=f32).astype(bf16)
    down_in = lax.all_to_all(down_part, DP, 0, 0, tiled=True)
    down_block = jnp.sum(
        down_in.reshape(count_dp, block_rows, down_in.shape[1]).astype(f32), axis=0
    )
    layer_out = (own_rows.astype(f32) + down_block).astype(bf16)

    row_ids = jnp.arange(total_rows, dtype=jnp.int32)
    ends = jnp.cumsum(state_len)
    starts = ends - state_len
    member = ((row_ids[:, None] >= starts[None, :]) & (row_ids[:, None] < ends[None, :])).astype(
        f32
    )
    importance = jnp.log1p(visits.astype(f32))
    per_state = total_rows * importance / (state_len.astype(f32) * jnp.sum(importance))
    row_weight = jnp.sum(member * per_state[None, :], axis=1)
    out_grad = (upstream.astype(f32) * row_weight[:, None]).astype(bf16)
    grad_down = lax.dot_general(
        hidden_all, out_grad, (((0,), (0,)), ((), ())), preferred_element_type=f32
    ).astype(bf16)
    hidden_term = lax.dot_general(
        out_grad, w_down, (((1,), (1,)), ((), ())), preferred_element_type=f32
    ).astype(bf16)
    grad_hidden = lax.psum(hidden_term, MP).astype(f32)
    sigmoid_gate = jax.nn.sigmoid(gate_all)
    gate_delta = (
        inverse[:, None]
        * grad_hidden
        * up_all
        * sigmoid_gate
        * (1.0 + gate_all * (1.0 - sigmoid_gate))
    ).astype(bf16)
    up_delta = (inverse[:, None] * grad_hidden * gate_all * sigmoid_gate).astype(bf16)
    grad_gate = lax.dot_general(
        scaled, gate_delta, (((0,), (0,)), ((), ())), preferred_element_type=f32
    ).astype(bf16)
    grad_up = lax.dot_general(
        scaled, up_delta, (((0,), (0,)), ((), ())), preferred_element_type=f32
    ).astype(bf16)
    return (layer_out, grad_gate, grad_up, grad_down)


def solution(mesh):
    sizes = dict(zip(mesh.axis_names, mesh.devices.shape))
    count_mp = sizes["mp"]
    count_dp = sizes["dp"]
    zh = 2
    y = 4
    x = count_dp // (zh * y)
    c = 2
    zl = count_mp // c
    view = Mesh(mesh.devices.reshape(x, zh, y, zl, c), DP + MP)
    in_specs = (
        P(DP, MP),
        P(),
        P(),
        P(),
        P(),
        P(MP),
        P(MP, DP),
        P(MP, DP),
        P(DP, MP),
        P(None, MP),
    )
    out_specs = (P(DP, MP), P(MP, DP), P(MP, DP), P(DP, MP))
    return jax.shard_map(body, mesh=view, in_specs=in_specs, out_specs=out_specs, check_vma=False)
```

```python
import jax
import jax.numpy as jnp
from jax import lax
from jax.sharding import Mesh
from jax.sharding import PartitionSpec as P


D = 8192

epsilon = 1e-05

DP = ("x", "zh", "y")
MP = ("zl", "c")


def ring_gather(piece, name):
    count = lax.axis_size(name)
    here = lax.axis_index(name)
    ahead = [(i, (i + 1) % count) for i in range(count)]
    behind = [(i, (i - 1) % count) for i in range(count)]
    parts = [piece]
    from_left = piece
    from_right = piece
    for step in range(1, count // 2 + 1):
        from_left = lax.ppermute(from_left, name, ahead)
        parts.append(from_left)
        if step < count - step:
            from_right = lax.ppermute(from_right, name, behind)
            parts.append(from_right)
    order = [0] * count
    order[0] = 0
    k = 1
    for step in range(1, count // 2 + 1):
        order[(count - step) % count] = k
        k += 1
        if step < count - step:
            order[step] = k
            k += 1
    stacked = jnp.stack([parts[order[j]] for j in range(count)])
    gathered = jnp.roll(stacked, here, axis=0)
    return gathered.reshape((count * piece.shape[0],) + piece.shape[1:])


def body(
    store_rows, source_shard, source_row, state_len, visits, gain, w_gate, w_up, w_down, upstream
):
    f32, bf16 = jnp.float32, jnp.bfloat16
    count_dp = 1
    for name in DP:
        count_dp *= lax.axis_size(name)
    index_dp = lax.axis_index(DP)
    total_rows = source_shard.shape[0]
    block_rows = total_rows // count_dp
    pair_cap = max(block_rows // 8, 1)
    store_dev = store_rows.shape[0]
    hidden_dev = w_gate.shape[1]

    shard = source_shard.reshape(count_dp, block_rows)
    srow = source_row.reshape(count_dp, block_rows)
    same = shard[:, :, None] == shard[:, None, :]
    t_ids = jnp.arange(block_rows, dtype=jnp.int32)
    earlier = t_ids[None, :] < t_ids[:, None]
    rank = jnp.sum((same & earlier[None]).astype(jnp.int32), axis=2)

    owned = shard == index_dp
    slots = jnp.arange(pair_cap, dtype=jnp.int32)
    hit = owned[:, :, None] & (rank[:, :, None] == slots[None, None, :])
    slot_row = jnp.sum(jnp.where(hit, srow[:, :, None] + 1, 0), axis=1) - 1
    pick_out = (
        slot_row.reshape(count_dp * pair_cap)[:, None]
        == jnp.arange(store_dev, dtype=jnp.int32)[None, :]
    ).astype(bf16)
    outgoing = jnp.dot(pick_out, store_rows, preferred_element_type=f32).astype(bf16)
    received = lax.all_to_all(outgoing, DP, 0, 0, tiled=True)

    my_shard = lax.dynamic_index_in_dim(shard, index_dp, 0, keepdims=False)
    my_rank = lax.dynamic_index_in_dim(rank, index_dp, 0, keepdims=False)
    pick_in = (
        (my_shard * pair_cap + my_rank)[:, None]
        == jnp.arange(count_dp * pair_cap, dtype=jnp.int32)[None, :]
    ).astype(bf16)
    own_rows = jnp.dot(pick_in, received, preferred_element_type=f32).astype(bf16)

    train_rows = own_rows
    for name in reversed(DP[1:]):
        train_rows = lax.all_gather(train_rows, name, axis=0, tiled=True)
    train_rows = ring_gather(train_rows, DP[0])

    row_ids = jnp.arange(total_rows, dtype=jnp.int32)
    ends = jnp.cumsum(state_len)
    starts = ends - state_len
    member = ((row_ids[:, None] >= starts[None, :]) & (row_ids[:, None] < ends[None, :])).astype(
        f32
    )
    importance = jnp.log1p(visits.astype(f32))
    per_state = total_rows * importance / (state_len.astype(f32) * jnp.sum(importance))
    row_weight = jnp.sum(member * per_state[None, :], axis=1)
    out_grad = (upstream.astype(f32) * row_weight[:, None]).astype(bf16)
    hidden_term = lax.dot_general(
        out_grad, w_down, (((1,), (1,)), ((), ())), preferred_element_type=f32
    ).astype(bf16)
    hidden_sum = lax.psum(hidden_term, MP)
    hidden_sum, train_rows = lax.optimization_barrier((hidden_sum, train_rows))
    grad_hidden = hidden_sum.astype(f32)

    rows_float = train_rows.astype(f32)
    squares = jnp.sum(rows_float * rows_float, axis=1)
    scaled = (rows_float * gain.astype(f32)[None, :]).astype(bf16)
    gate_term = jnp.dot(scaled, w_gate, preferred_element_type=f32)
    up_term = jnp.dot(scaled, w_up, preferred_element_type=f32)
    packed = jnp.concatenate([gate_term, up_term, squares[:, None]], axis=1).astype(bf16)
    total = lax.psum(packed, MP).astype(f32)
    gate_total = total[:, :hidden_dev]
    up_total = total[:, hidden_dev : 2 * hidden_dev]
    square_total = total[:, 2 * hidden_dev]
    inverse = lax.rsqrt(square_total / D + epsilon)
    gate_all = inverse[:, None] * gate_total
    up_all = inverse[:, None] * up_total
    hidden_all = (jax.nn.silu(gate_all) * up_all).astype(bf16)

    down_part = jnp.dot(hidden_all, w_down, preferred_element_type=f32).astype(bf16)
    down_in = lax.all_to_all(down_part, DP, 0, 0, tiled=True)
    down_block = jnp.sum(
        down_in.reshape(count_dp, block_rows, down_in.shape[1]).astype(f32), axis=0
    )
    layer_out = (own_rows.astype(f32) + down_block).astype(bf16)

    grad_down = lax.dot_general(
        hidden_all, out_grad, (((0,), (0,)), ((), ())), preferred_element_type=f32
    ).astype(bf16)
    sigmoid_gate = jax.nn.sigmoid(gate_all)
    gate_delta = (
        inverse[:, None]
        * grad_hidden
        * up_all
        * sigmoid_gate
        * (1.0 + gate_all * (1.0 - sigmoid_gate))
    ).astype(bf16)
    up_delta = (inverse[:, None] * grad_hidden * gate_all * sigmoid_gate).astype(bf16)
    grad_gate = lax.dot_general(
        scaled, gate_delta, (((0,), (0,)), ((), ())), preferred_element_type=f32
    ).astype(bf16)
    grad_up = lax.dot_general(
        scaled, up_delta, (((0,), (0,)), ((), ())), preferred_element_type=f32
    ).astype(bf16)
    return (layer_out, grad_gate, grad_up, grad_down)


def solution(mesh):
    sizes = dict(zip(mesh.axis_names, mesh.devices.shape))
    count_mp = sizes["mp"]
    count_dp = sizes["dp"]
    zh = 2
    y = 4
    x = count_dp // (zh * y)
    c = 2
    zl = count_mp // c
    view = Mesh(mesh.devices.reshape(x, zh, y, zl, c), DP + MP)
    in_specs = (
        P(DP, MP),
        P(),
        P(),
        P(),
        P(),
        P(MP),
        P(MP, DP),
        P(MP, DP),
        P(DP, MP),
        P(None, MP),
    )
    out_specs = (P(DP, MP), P(MP, DP), P(MP, DP), P(DP, MP))
    return jax.shard_map(body, mesh=view, in_specs=in_specs, out_specs=out_specs, check_vma=False)
```

```python
import jax
import jax.numpy as jnp
from jax import lax
from jax.sharding import Mesh
from jax.sharding import PartitionSpec as P


D = 8192

epsilon = 1e-05

DP = ("x", "zh", "y")
MP = ("zl", "c")


def ring_gather(piece, name):
    count = lax.axis_size(name)
    here = lax.axis_index(name)
    ahead = [(i, (i + 1) % count) for i in range(count)]
    behind = [(i, (i - 1) % count) for i in range(count)]
    parts = [piece]
    from_left = piece
    from_right = piece
    for step in range(1, count // 2 + 1):
        from_left = lax.ppermute(from_left, name, ahead)
        parts.append(from_left)
        if step < count - step:
            from_right = lax.ppermute(from_right, name, behind)
            parts.append(from_right)
    order = [0] * count
    order[0] = 0
    k = 1
    for step in range(1, count // 2 + 1):
        order[(count - step) % count] = k
        k += 1
        if step < count - step:
            order[step] = k
            k += 1
    stacked = jnp.stack([parts[order[j]] for j in range(count)])
    gathered = jnp.roll(stacked, here, axis=0)
    return gathered.reshape((count * piece.shape[0],) + piece.shape[1:])


def staged_scatter(part, block_rows):
    sizes = tuple(lax.axis_size(name) for name in DP)
    features = part.shape[1]
    held = part.reshape(sizes + (block_rows, features))
    held = jnp.transpose(held, (2, 0, 1, 3, 4))
    total = None
    for name in (DP[2], DP[0], DP[1]):
        arrived = lax.all_to_all(held, name, 0, 0, tiled=True)
        total = jnp.sum(arrived.astype(jnp.float32), axis=0)
        held = total.astype(part.dtype)
    return total.reshape(block_rows, features)


def body(
    store_rows, source_shard, source_row, state_len, visits, gain, w_gate, w_up, w_down, upstream
):
    f32, bf16 = jnp.float32, jnp.bfloat16
    count_dp = 1
    for name in DP:
        count_dp *= lax.axis_size(name)
    index_dp = lax.axis_index(DP)
    total_rows = source_shard.shape[0]
    block_rows = total_rows // count_dp
    pair_cap = max(block_rows // 8, 1)
    store_dev = store_rows.shape[0]
    hidden_dev = w_gate.shape[1]

    shard = source_shard.reshape(count_dp, block_rows)
    srow = source_row.reshape(count_dp, block_rows)
    same = shard[:, :, None] == shard[:, None, :]
    t_ids = jnp.arange(block_rows, dtype=jnp.int32)
    earlier = t_ids[None, :] < t_ids[:, None]
    rank = jnp.sum((same & earlier[None]).astype(jnp.int32), axis=2)

    owned = shard == index_dp
    slots = jnp.arange(pair_cap, dtype=jnp.int32)
    hit = owned[:, :, None] & (rank[:, :, None] == slots[None, None, :])
    slot_row = jnp.sum(jnp.where(hit, srow[:, :, None] + 1, 0), axis=1) - 1
    pick_out = (
        slot_row.reshape(count_dp * pair_cap)[:, None]
        == jnp.arange(store_dev, dtype=jnp.int32)[None, :]
    ).astype(bf16)
    outgoing = jnp.dot(pick_out, store_rows, preferred_element_type=f32).astype(bf16)
    received = lax.all_to_all(outgoing, DP, 0, 0, tiled=True)

    my_shard = lax.dynamic_index_in_dim(shard, index_dp, 0, keepdims=False)
    my_rank = lax.dynamic_index_in_dim(rank, index_dp, 0, keepdims=False)
    pick_in = (
        (my_shard * pair_cap + my_rank)[:, None]
        == jnp.arange(count_dp * pair_cap, dtype=jnp.int32)[None, :]
    ).astype(bf16)
    own_rows = jnp.dot(pick_in, received, preferred_element_type=f32).astype(bf16)

    train_rows = own_rows
    for name in reversed(DP[1:]):
        train_rows = lax.all_gather(train_rows, name, axis=0, tiled=True)
    train_rows = ring_gather(train_rows, DP[0])

    row_ids = jnp.arange(total_rows, dtype=jnp.int32)
    ends = jnp.cumsum(state_len)
    starts = ends - state_len
    member = ((row_ids[:, None] >= starts[None, :]) & (row_ids[:, None] < ends[None, :])).astype(
        f32
    )
    importance = jnp.log1p(visits.astype(f32))
    per_state = total_rows * importance / (state_len.astype(f32) * jnp.sum(importance))
    row_weight = jnp.sum(member * per_state[None, :], axis=1)
    out_grad = (upstream.astype(f32) * row_weight[:, None]).astype(bf16)
    hidden_term = lax.dot_general(
        out_grad, w_down, (((1,), (1,)), ((), ())), preferred_element_type=f32
    ).astype(bf16)
    hidden_sum = lax.psum(hidden_term, MP)
    hidden_sum, train_rows = lax.optimization_barrier((hidden_sum, train_rows))
    grad_hidden = hidden_sum.astype(f32)

    rows_float = train_rows.astype(f32)
    squares = jnp.sum(rows_float * rows_float, axis=1)
    scaled = (rows_float * gain.astype(f32)[None, :]).astype(bf16)
    gate_term = jnp.dot(scaled, w_gate, preferred_element_type=f32)
    up_term = jnp.dot(scaled, w_up, preferred_element_type=f32)
    packed = jnp.concatenate([gate_term, up_term, squares[:, None]], axis=1).astype(bf16)
    total = lax.psum(packed, MP).astype(f32)
    gate_total = total[:, :hidden_dev]
    up_total = total[:, hidden_dev : 2 * hidden_dev]
    square_total = total[:, 2 * hidden_dev]
    inverse = lax.rsqrt(square_total / D + epsilon)
    gate_all = inverse[:, None] * gate_total
    up_all = inverse[:, None] * up_total
    hidden_all = (jax.nn.silu(gate_all) * up_all).astype(bf16)

    down_part = jnp.dot(hidden_all, w_down, preferred_element_type=f32).astype(bf16)
    down_block = staged_scatter(down_part, block_rows)
    layer_out = (own_rows.astype(f32) + down_block).astype(bf16)

    grad_down = lax.dot_general(
        hidden_all, out_grad, (((0,), (0,)), ((), ())), preferred_element_type=f32
    ).astype(bf16)
    sigmoid_gate = jax.nn.sigmoid(gate_all)
    gate_delta = (
        inverse[:, None]
        * grad_hidden
        * up_all
        * sigmoid_gate
        * (1.0 + gate_all * (1.0 - sigmoid_gate))
    ).astype(bf16)
    up_delta = (inverse[:, None] * grad_hidden * gate_all * sigmoid_gate).astype(bf16)
    grad_gate = lax.dot_general(
        scaled, gate_delta, (((0,), (0,)), ((), ())), preferred_element_type=f32
    ).astype(bf16)
    grad_up = lax.dot_general(
        scaled, up_delta, (((0,), (0,)), ((), ())), preferred_element_type=f32
    ).astype(bf16)
    return (layer_out, grad_gate, grad_up, grad_down)


def solution(mesh):
    sizes = dict(zip(mesh.axis_names, mesh.devices.shape))
    count_mp = sizes["mp"]
    count_dp = sizes["dp"]
    zh = 2
    y = 4
    x = count_dp // (zh * y)
    c = 2
    zl = count_mp // c
    view = Mesh(mesh.devices.reshape(x, zh, y, zl, c), DP + MP)
    in_specs = (
        P(DP, MP),
        P(),
        P(),
        P(),
        P(),
        P(MP),
        P(MP, DP),
        P(MP, DP),
        P(DP, MP),
        P(None, MP),
    )
    out_specs = (P(DP, MP), P(MP, DP), P(MP, DP), P(DP, MP))
    return jax.shard_map(body, mesh=view, in_specs=in_specs, out_specs=out_specs, check_vma=False)
```

```python
import jax
import jax.numpy as jnp
from jax import lax
from jax.sharding import Mesh
from jax.sharding import PartitionSpec as P


D = 8192

epsilon = 1e-05

DP = ("x", "zh", "y")
MP = ("zl", "c")


def ring_gather(piece, name):
    count = lax.axis_size(name)
    here = lax.axis_index(name)
    ahead = [(i, (i + 1) % count) for i in range(count)]
    behind = [(i, (i - 1) % count) for i in range(count)]
    parts = [piece]
    from_left = piece
    from_right = piece
    for step in range(1, count // 2 + 1):
        from_left = lax.ppermute(from_left, name, ahead)
        parts.append(from_left)
        if step < count - step:
            from_right = lax.ppermute(from_right, name, behind)
            parts.append(from_right)
    order = [0] * count
    order[0] = 0
    k = 1
    for step in range(1, count // 2 + 1):
        order[(count - step) % count] = k
        k += 1
        if step < count - step:
            order[step] = k
            k += 1
    stacked = jnp.stack([parts[order[j]] for j in range(count)])
    gathered = jnp.roll(stacked, here, axis=0)
    return gathered.reshape((count * piece.shape[0],) + piece.shape[1:])


def staged_scatter(part, block_rows):
    sizes = tuple(lax.axis_size(name) for name in DP)
    features = part.shape[1]
    held = part.reshape(sizes + (block_rows, features))
    held = jnp.transpose(held, (2, 0, 1, 3, 4))
    total = None
    for name in (DP[2], DP[0], DP[1]):
        arrived = lax.all_to_all(held, name, 0, 0, tiled=True)
        total = jnp.sum(arrived.astype(jnp.float32), axis=0)
        held = total.astype(part.dtype)
    return total.reshape(block_rows, features)


def pair_allreduce(part, names):
    steps = []
    for name in reversed(names):
        count = lax.axis_size(name)
        bit = 1
        while bit < count:
            steps.append((name, bit))
            bit *= 2
    held = part.astype(jnp.float32)
    for name, bit in steps:
        pairs = [(i, i ^ bit) for i in range(lax.axis_size(name))]
        upper = (lax.axis_index(name) & bit) != 0
        low, high = jnp.split(held, 2, axis=0)
        keep = jnp.where(upper, high, low)
        give = jnp.where(upper, low, high)
        got = lax.ppermute(give.astype(part.dtype), name, pairs)
        held = keep + got.astype(jnp.float32)
    held = held.astype(part.dtype)
    for name, bit in reversed(steps):
        pairs = [(i, i ^ bit) for i in range(lax.axis_size(name))]
        upper = (lax.axis_index(name) & bit) != 0
        got = lax.ppermute(held, name, pairs)
        held = jnp.where(
            upper, jnp.concatenate([got, held], axis=0), jnp.concatenate([held, got], axis=0)
        )
    return held


def body(
    store_rows, source_shard, source_row, state_len, visits, gain, w_gate, w_up, w_down, upstream
):
    f32, bf16 = jnp.float32, jnp.bfloat16
    count_dp = 1
    for name in DP:
        count_dp *= lax.axis_size(name)
    index_dp = lax.axis_index(DP)
    total_rows = source_shard.shape[0]
    block_rows = total_rows // count_dp
    pair_cap = max(block_rows // 8, 1)
    store_dev = store_rows.shape[0]
    hidden_dev = w_gate.shape[1]

    shard = source_shard.reshape(count_dp, block_rows)
    srow = source_row.reshape(count_dp, block_rows)
    same = shard[:, :, None] == shard[:, None, :]
    t_ids = jnp.arange(block_rows, dtype=jnp.int32)
    earlier = t_ids[None, :] < t_ids[:, None]
    rank = jnp.sum((same & earlier[None]).astype(jnp.int32), axis=2)

    owned = shard == index_dp
    slots = jnp.arange(pair_cap, dtype=jnp.int32)
    hit = owned[:, :, None] & (rank[:, :, None] == slots[None, None, :])
    slot_row = jnp.sum(jnp.where(hit, srow[:, :, None] + 1, 0), axis=1) - 1
    pick_out = (
        slot_row.reshape(count_dp * pair_cap)[:, None]
        == jnp.arange(store_dev, dtype=jnp.int32)[None, :]
    ).astype(bf16)
    outgoing = jnp.dot(pick_out, store_rows, preferred_element_type=f32).astype(bf16)
    received = lax.all_to_all(outgoing, DP, 0, 0, tiled=True)

    my_shard = lax.dynamic_index_in_dim(shard, index_dp, 0, keepdims=False)
    my_rank = lax.dynamic_index_in_dim(rank, index_dp, 0, keepdims=False)
    pick_in = (
        (my_shard * pair_cap + my_rank)[:, None]
        == jnp.arange(count_dp * pair_cap, dtype=jnp.int32)[None, :]
    ).astype(bf16)
    own_rows = jnp.dot(pick_in, received, preferred_element_type=f32).astype(bf16)

    train_rows = own_rows
    for name in reversed(DP):
        train_rows = ring_gather(train_rows, name)

    row_ids = jnp.arange(total_rows, dtype=jnp.int32)
    ends = jnp.cumsum(state_len)
    starts = ends - state_len
    member = ((row_ids[:, None] >= starts[None, :]) & (row_ids[:, None] < ends[None, :])).astype(
        f32
    )
    importance = jnp.log1p(visits.astype(f32))
    per_state = total_rows * importance / (state_len.astype(f32) * jnp.sum(importance))
    row_weight = jnp.sum(member * per_state[None, :], axis=1)
    out_grad = (upstream.astype(f32) * row_weight[:, None]).astype(bf16)
    hidden_term = lax.dot_general(
        out_grad, w_down, (((1,), (1,)), ((), ())), preferred_element_type=f32
    ).astype(bf16)
    hidden_sum = pair_allreduce(hidden_term, MP)
    grad_hidden = hidden_sum.astype(f32)

    rows_float = train_rows.astype(f32)
    squares = jnp.sum(rows_float * rows_float, axis=1)
    scaled = (rows_float * gain.astype(f32)[None, :]).astype(bf16)
    gate_term = jnp.dot(scaled, w_gate, preferred_element_type=f32)
    up_term = jnp.dot(scaled, w_up, preferred_element_type=f32)
    packed = jnp.concatenate([gate_term, up_term, squares[:, None]], axis=1).astype(bf16)
    total = lax.psum(packed, MP).astype(f32)
    gate_total = total[:, :hidden_dev]
    up_total = total[:, hidden_dev : 2 * hidden_dev]
    square_total = total[:, 2 * hidden_dev]
    inverse = lax.rsqrt(square_total / D + epsilon)
    gate_all = inverse[:, None] * gate_total
    up_all = inverse[:, None] * up_total
    hidden_all = (jax.nn.silu(gate_all) * up_all).astype(bf16)

    down_part = jnp.dot(hidden_all, w_down, preferred_element_type=f32).astype(bf16)
    down_block = staged_scatter(down_part, block_rows)
    layer_out = (own_rows.astype(f32) + down_block).astype(bf16)

    grad_down = lax.dot_general(
        hidden_all, out_grad, (((0,), (0,)), ((), ())), preferred_element_type=f32
    ).astype(bf16)
    sigmoid_gate = jax.nn.sigmoid(gate_all)
    gate_delta = (
        inverse[:, None]
        * grad_hidden
        * up_all
        * sigmoid_gate
        * (1.0 + gate_all * (1.0 - sigmoid_gate))
    ).astype(bf16)
    up_delta = (inverse[:, None] * grad_hidden * gate_all * sigmoid_gate).astype(bf16)
    grad_gate = lax.dot_general(
        scaled, gate_delta, (((0,), (0,)), ((), ())), preferred_element_type=f32
    ).astype(bf16)
    grad_up = lax.dot_general(
        scaled, up_delta, (((0,), (0,)), ((), ())), preferred_element_type=f32
    ).astype(bf16)
    return (layer_out, grad_gate, grad_up, grad_down)


def solution(mesh):
    sizes = dict(zip(mesh.axis_names, mesh.devices.shape))
    count_mp = sizes["mp"]
    count_dp = sizes["dp"]
    zh = 2
    y = 4
    x = count_dp // (zh * y)
    c = 2
    zl = count_mp // c
    view = Mesh(mesh.devices.reshape(x, zh, y, zl, c), DP + MP)
    in_specs = (
        P(DP, MP),
        P(),
        P(),
        P(),
        P(),
        P(MP),
        P(MP, DP),
        P(MP, DP),
        P(DP, MP),
        P(None, MP),
    )
    out_specs = (P(DP, MP), P(MP, DP), P(MP, DP), P(DP, MP))
    return jax.shard_map(body, mesh=view, in_specs=in_specs, out_specs=out_specs, check_vma=False)
```

```python
import jax
import jax.numpy as jnp
from jax import lax
from jax.sharding import Mesh
from jax.sharding import PartitionSpec as P


D = 8192

epsilon = 1e-05

DP = ("x", "zh", "y")
MP = ("zl", "c")


def ring_gather(piece, name):
    count = lax.axis_size(name)
    here = lax.axis_index(name)
    ahead = [(i, (i + 1) % count) for i in range(count)]
    behind = [(i, (i - 1) % count) for i in range(count)]
    parts = [piece]
    from_left = piece
    from_right = piece
    for step in range(1, count // 2 + 1):
        from_left = lax.ppermute(from_left, name, ahead)
        parts.append(from_left)
        if step < count - step:
            from_right = lax.ppermute(from_right, name, behind)
            parts.append(from_right)
    order = [0] * count
    order[0] = 0
    k = 1
    for step in range(1, count // 2 + 1):
        order[(count - step) % count] = k
        k += 1
        if step < count - step:
            order[step] = k
            k += 1
    stacked = jnp.stack([parts[order[j]] for j in range(count)])
    gathered = jnp.roll(stacked, here, axis=0)
    return gathered.reshape((count * piece.shape[0],) + piece.shape[1:])


def staged_scatter(part, block_rows):
    sizes = tuple(lax.axis_size(name) for name in DP)
    features = part.shape[1]
    held = part.reshape(sizes + (block_rows, features))
    held = jnp.transpose(held, (2, 0, 1, 3, 4))
    total = None
    for name in (DP[2], DP[0], DP[1]):
        arrived = lax.all_to_all(held, name, 0, 0, tiled=True)
        total = jnp.sum(arrived.astype(jnp.float32), axis=0)
        held = total.astype(part.dtype)
    return total.reshape(block_rows, features)


def pair_allreduce(part, names):
    steps = []
    for name in reversed(names):
        count = lax.axis_size(name)
        bit = 1
        while bit < count:
            steps.append((name, bit))
            bit *= 2
    held = part.astype(jnp.float32)
    for name, bit in steps:
        pairs = [(i, i ^ bit) for i in range(lax.axis_size(name))]
        upper = (lax.axis_index(name) & bit) != 0
        low, high = jnp.split(held, 2, axis=0)
        keep = jnp.where(upper, high, low)
        give = jnp.where(upper, low, high)
        got = lax.ppermute(give.astype(part.dtype), name, pairs)
        held = keep + got.astype(jnp.float32)
    held = held.astype(part.dtype)
    for name, bit in reversed(steps):
        pairs = [(i, i ^ bit) for i in range(lax.axis_size(name))]
        upper = (lax.axis_index(name) & bit) != 0
        got = lax.ppermute(held, name, pairs)
        held = jnp.where(
            upper, jnp.concatenate([got, held], axis=0), jnp.concatenate([held, got], axis=0)
        )
    return held


def body(
    store_rows, source_shard, source_row, state_len, visits, gain, w_gate, w_up, w_down, upstream
):
    f32, bf16 = jnp.float32, jnp.bfloat16
    count_dp = 1
    for name in DP:
        count_dp *= lax.axis_size(name)
    index_dp = lax.axis_index(DP)
    total_rows = source_shard.shape[0]
    block_rows = total_rows // count_dp
    pair_cap = max(block_rows // 8, 1)
    store_dev = store_rows.shape[0]
    hidden_dev = w_gate.shape[1]

    shard = source_shard.reshape(count_dp, block_rows)
    srow = source_row.reshape(count_dp, block_rows)
    same = shard[:, :, None] == shard[:, None, :]
    t_ids = jnp.arange(block_rows, dtype=jnp.int32)
    earlier = t_ids[None, :] < t_ids[:, None]
    rank = jnp.sum((same & earlier[None]).astype(jnp.int32), axis=2)

    owned = shard == index_dp
    slots = jnp.arange(pair_cap, dtype=jnp.int32)
    hit = owned[:, :, None] & (rank[:, :, None] == slots[None, None, :])
    slot_row = jnp.sum(jnp.where(hit, srow[:, :, None] + 1, 0), axis=1) - 1
    pick_out = (
        slot_row.reshape(count_dp * pair_cap)[:, None]
        == jnp.arange(store_dev, dtype=jnp.int32)[None, :]
    ).astype(bf16)
    outgoing = jnp.dot(pick_out, store_rows, preferred_element_type=f32).astype(bf16)
    received = lax.all_to_all(outgoing, DP, 0, 0, tiled=True)

    my_shard = lax.dynamic_index_in_dim(shard, index_dp, 0, keepdims=False)
    my_rank = lax.dynamic_index_in_dim(rank, index_dp, 0, keepdims=False)
    pick_in = (
        (my_shard * pair_cap + my_rank)[:, None]
        == jnp.arange(count_dp * pair_cap, dtype=jnp.int32)[None, :]
    ).astype(bf16)
    own_rows = jnp.dot(pick_in, received, preferred_element_type=f32).astype(bf16)

    train_rows = own_rows
    for name in reversed(DP):
        train_rows = ring_gather(train_rows, name)

    row_ids = jnp.arange(total_rows, dtype=jnp.int32)
    ends = jnp.cumsum(state_len)
    starts = ends - state_len
    member = ((row_ids[:, None] >= starts[None, :]) & (row_ids[:, None] < ends[None, :])).astype(
        f32
    )
    importance = jnp.log1p(visits.astype(f32))
    per_state = total_rows * importance / (state_len.astype(f32) * jnp.sum(importance))
    row_weight = jnp.sum(member * per_state[None, :], axis=1)
    out_grad = (upstream.astype(f32) * row_weight[:, None]).astype(bf16)
    hidden_term = lax.dot_general(
        out_grad, w_down, (((1,), (1,)), ((), ())), preferred_element_type=f32
    ).astype(bf16)
    hidden_sum = lax.psum(hidden_term, MP)
    hidden_sum, train_rows = lax.optimization_barrier((hidden_sum, train_rows))
    grad_hidden = hidden_sum.astype(f32)

    rows_float = train_rows.astype(f32)
    squares = jnp.sum(rows_float * rows_float, axis=1)
    scaled = (rows_float * gain.astype(f32)[None, :]).astype(bf16)
    gate_term = jnp.dot(scaled, w_gate, preferred_element_type=f32)
    up_term = jnp.dot(scaled, w_up, preferred_element_type=f32)
    packed = jnp.concatenate([gate_term, up_term, squares[:, None]], axis=1).astype(bf16)
    total = pair_allreduce(packed, MP).astype(f32)
    gate_total = total[:, :hidden_dev]
    up_total = total[:, hidden_dev : 2 * hidden_dev]
    square_total = total[:, 2 * hidden_dev]
    inverse = lax.rsqrt(square_total / D + epsilon)
    gate_all = inverse[:, None] * gate_total
    up_all = inverse[:, None] * up_total
    hidden_all = (jax.nn.silu(gate_all) * up_all).astype(bf16)

    down_part = jnp.dot(hidden_all, w_down, preferred_element_type=f32).astype(bf16)
    down_block = staged_scatter(down_part, block_rows)
    layer_out = (own_rows.astype(f32) + down_block).astype(bf16)

    grad_down = lax.dot_general(
        hidden_all, out_grad, (((0,), (0,)), ((), ())), preferred_element_type=f32
    ).astype(bf16)
    sigmoid_gate = jax.nn.sigmoid(gate_all)
    gate_delta = (
        inverse[:, None]
        * grad_hidden
        * up_all
        * sigmoid_gate
        * (1.0 + gate_all * (1.0 - sigmoid_gate))
    ).astype(bf16)
    up_delta = (inverse[:, None] * grad_hidden * gate_all * sigmoid_gate).astype(bf16)
    grad_gate = lax.dot_general(
        scaled, gate_delta, (((0,), (0,)), ((), ())), preferred_element_type=f32
    ).astype(bf16)
    grad_up = lax.dot_general(
        scaled, up_delta, (((0,), (0,)), ((), ())), preferred_element_type=f32
    ).astype(bf16)
    return (layer_out, grad_gate, grad_up, grad_down)


def solution(mesh):
    sizes = dict(zip(mesh.axis_names, mesh.devices.shape))
    count_mp = sizes["mp"]
    count_dp = sizes["dp"]
    zh = 2
    y = 4
    x = count_dp // (zh * y)
    c = 2
    zl = count_mp // c
    view = Mesh(mesh.devices.reshape(x, zh, y, zl, c), DP + MP)
    in_specs = (
        P(DP, MP),
        P(),
        P(),
        P(),
        P(),
        P(MP),
        P(MP, DP),
        P(MP, DP),
        P(DP, MP),
        P(None, MP),
    )
    out_specs = (P(DP, MP), P(MP, DP), P(MP, DP), P(DP, MP))
    return jax.shard_map(body, mesh=view, in_specs=in_specs, out_specs=out_specs, check_vma=False)
```

```python
import jax
import jax.numpy as jnp
from jax import lax
from jax.sharding import Mesh
from jax.sharding import PartitionSpec as P


D = 8192

epsilon = 1e-05

DP = ("x", "zh", "y")
MP = ("zl", "c")


def ring_gather(piece, name):
    count = lax.axis_size(name)
    here = lax.axis_index(name)
    ahead = [(i, (i + 1) % count) for i in range(count)]
    behind = [(i, (i - 1) % count) for i in range(count)]
    parts = [piece]
    from_left = piece
    from_right = piece
    for step in range(1, count // 2 + 1):
        from_left = lax.ppermute(from_left, name, ahead)
        parts.append(from_left)
        if step < count - step:
            from_right = lax.ppermute(from_right, name, behind)
            parts.append(from_right)
    order = [0] * count
    order[0] = 0
    k = 1
    for step in range(1, count // 2 + 1):
        order[(count - step) % count] = k
        k += 1
        if step < count - step:
            order[step] = k
            k += 1
    stacked = jnp.stack([parts[order[j]] for j in range(count)])
    gathered = jnp.roll(stacked, here, axis=0)
    return gathered.reshape((count * piece.shape[0],) + piece.shape[1:])


def staged_scatter(part, block_rows):
    sizes = tuple(lax.axis_size(name) for name in DP)
    features = part.shape[1]
    held = part.reshape(sizes + (block_rows, features))
    held = jnp.transpose(held, (2, 0, 1, 3, 4))
    total = None
    for name in (DP[2], DP[0], DP[1]):
        arrived = lax.all_to_all(held, name, 0, 0, tiled=True)
        total = jnp.sum(arrived.astype(jnp.float32), axis=0)
        held = total.astype(part.dtype)
    return total.reshape(block_rows, features)


def pair_allreduce(part, names):
    steps = []
    for name in reversed(names):
        count = lax.axis_size(name)
        bit = 1
        while bit < count:
            steps.append((name, bit))
            bit *= 2
    held = part.astype(jnp.float32)
    for name, bit in steps:
        pairs = [(i, i ^ bit) for i in range(lax.axis_size(name))]
        upper = (lax.axis_index(name) & bit) != 0
        low, high = jnp.split(held, 2, axis=0)
        keep = jnp.where(upper, high, low)
        give = jnp.where(upper, low, high)
        got = lax.ppermute(give.astype(part.dtype), name, pairs)
        held = keep + got.astype(jnp.float32)
    held = held.astype(part.dtype)
    for name, bit in reversed(steps):
        pairs = [(i, i ^ bit) for i in range(lax.axis_size(name))]
        upper = (lax.axis_index(name) & bit) != 0
        got = lax.ppermute(held, name, pairs)
        held = jnp.where(
            upper, jnp.concatenate([got, held], axis=0), jnp.concatenate([held, got], axis=0)
        )
    return held


def halves(rows, blocks):
    shaped = rows.reshape((blocks, 2, rows.shape[0] // (2 * blocks)) + rows.shape[1:])
    return jnp.swapaxes(shaped, 0, 1).reshape(rows.shape)


def body(
    store_rows, source_shard, source_row, state_len, visits, gain, w_gate, w_up, w_down, upstream
):
    f32, bf16 = jnp.float32, jnp.bfloat16
    count_dp = 1
    for name in DP:
        count_dp *= lax.axis_size(name)
    index_dp = lax.axis_index(DP)
    total_rows = source_shard.shape[0]
    block_rows = total_rows // count_dp
    pair_cap = max(block_rows // 8, 1)
    store_dev = store_rows.shape[0]
    hidden_dev = w_gate.shape[1]

    shard = source_shard.reshape(count_dp, block_rows)
    srow = source_row.reshape(count_dp, block_rows)
    same = shard[:, :, None] == shard[:, None, :]
    t_ids = jnp.arange(block_rows, dtype=jnp.int32)
    earlier = t_ids[None, :] < t_ids[:, None]
    rank = jnp.sum((same & earlier[None]).astype(jnp.int32), axis=2)

    owned = shard == index_dp
    slots = jnp.arange(pair_cap, dtype=jnp.int32)
    hit = owned[:, :, None] & (rank[:, :, None] == slots[None, None, :])
    slot_row = jnp.sum(jnp.where(hit, srow[:, :, None] + 1, 0), axis=1) - 1
    pick_out = (
        slot_row.reshape(count_dp * pair_cap)[:, None]
        == jnp.arange(store_dev, dtype=jnp.int32)[None, :]
    ).astype(bf16)
    outgoing = jnp.dot(pick_out, store_rows, preferred_element_type=f32).astype(bf16)
    received = lax.all_to_all(outgoing, DP, 0, 0, tiled=True)

    my_shard = lax.dynamic_index_in_dim(shard, index_dp, 0, keepdims=False)
    my_rank = lax.dynamic_index_in_dim(rank, index_dp, 0, keepdims=False)
    pick_in = (
        (my_shard * pair_cap + my_rank)[:, None]
        == jnp.arange(count_dp * pair_cap, dtype=jnp.int32)[None, :]
    ).astype(bf16)
    own_rows = jnp.dot(pick_in, received, preferred_element_type=f32).astype(bf16)

    train_rows = own_rows
    for name in reversed(DP):
        train_rows = ring_gather(train_rows, name)

    row_ids = jnp.arange(total_rows, dtype=jnp.int32)
    ends = jnp.cumsum(state_len)
    starts = ends - state_len
    member = ((row_ids[:, None] >= starts[None, :]) & (row_ids[:, None] < ends[None, :])).astype(
        f32
    )
    importance = jnp.log1p(visits.astype(f32))
    per_state = total_rows * importance / (state_len.astype(f32) * jnp.sum(importance))
    row_weight = jnp.sum(member * per_state[None, :], axis=1)
    out_grad = halves((upstream.astype(f32) * row_weight[:, None]).astype(bf16), count_dp)
    hidden_term = lax.dot_general(
        out_grad, w_down, (((1,), (1,)), ((), ())), preferred_element_type=f32
    ).astype(bf16)
    hidden_sum = lax.psum(hidden_term, MP)
    train_rows = halves(train_rows, count_dp)
    hidden_sum, train_rows = lax.optimization_barrier((hidden_sum, train_rows))
    grad_hidden = hidden_sum.astype(f32)

    rows_float = train_rows.astype(f32)
    squares = jnp.sum(rows_float * rows_float, axis=1)
    scaled = (rows_float * gain.astype(f32)[None, :]).astype(bf16)
    gate_term = jnp.dot(scaled, w_gate, preferred_element_type=f32)
    up_term = jnp.dot(scaled, w_up, preferred_element_type=f32)
    packed = jnp.concatenate([gate_term, up_term, squares[:, None]], axis=1).astype(bf16)
    chunk = total_rows // 2
    pieces = []
    later = packed[chunk:]
    for first in (0, chunk):
        reduced = pair_allreduce(packed[:chunk] if first == 0 else later, MP)
        if first == 0:
            reduced, later = lax.optimization_barrier((reduced, later))
        part_total = reduced.astype(f32)
        part_inverse = lax.rsqrt(part_total[:, 2 * hidden_dev] / D + epsilon)
        part_gate = part_inverse[:, None] * part_total[:, :hidden_dev]
        part_up = part_inverse[:, None] * part_total[:, hidden_dev : 2 * hidden_dev]
        part_hidden = (jax.nn.silu(part_gate) * part_up).astype(bf16)
        down_part = jnp.dot(part_hidden, w_down, preferred_element_type=f32).astype(bf16)
        down_rows = staged_scatter(down_part, block_rows // 2)
        pieces.append((part_inverse, part_gate, part_up, part_hidden, down_rows))
    inverse = jnp.concatenate([p[0] for p in pieces], axis=0)
    gate_all = jnp.concatenate([p[1] for p in pieces], axis=0)
    up_all = jnp.concatenate([p[2] for p in pieces], axis=0)
    hidden_all = jnp.concatenate([p[3] for p in pieces], axis=0)
    down_block = jnp.concatenate([p[4] for p in pieces], axis=0)
    layer_out = (own_rows.astype(f32) + down_block).astype(bf16)

    grad_down = lax.dot_general(
        hidden_all, out_grad, (((0,), (0,)), ((), ())), preferred_element_type=f32
    ).astype(bf16)
    sigmoid_gate = jax.nn.sigmoid(gate_all)
    gate_delta = (
        inverse[:, None]
        * grad_hidden
        * up_all
        * sigmoid_gate
        * (1.0 + gate_all * (1.0 - sigmoid_gate))
    ).astype(bf16)
    up_delta = (inverse[:, None] * grad_hidden * gate_all * sigmoid_gate).astype(bf16)
    grad_gate = lax.dot_general(
        scaled, gate_delta, (((0,), (0,)), ((), ())), preferred_element_type=f32
    ).astype(bf16)
    grad_up = lax.dot_general(
        scaled, up_delta, (((0,), (0,)), ((), ())), preferred_element_type=f32
    ).astype(bf16)
    return (layer_out, grad_gate, grad_up, grad_down)


def solution(mesh):
    sizes = dict(zip(mesh.axis_names, mesh.devices.shape))
    count_mp = sizes["mp"]
    count_dp = sizes["dp"]
    zh = 2
    y = 4
    x = count_dp // (zh * y)
    c = 2
    zl = count_mp // c
    view = Mesh(mesh.devices.reshape(x, zh, y, zl, c), DP + MP)
    in_specs = (
        P(DP, MP),
        P(),
        P(),
        P(),
        P(),
        P(MP),
        P(MP, DP),
        P(MP, DP),
        P(DP, MP),
        P(None, MP),
    )
    out_specs = (P(DP, MP), P(MP, DP), P(MP, DP), P(DP, MP))
    return jax.shard_map(body, mesh=view, in_specs=in_specs, out_specs=out_specs, check_vma=False)
```

```python
import jax
import jax.numpy as jnp
from jax import lax
from jax.sharding import Mesh
from jax.sharding import PartitionSpec as P


D = 8192

epsilon = 1e-05

DP = ("x", "zh", "y")
MP = ("zl", "c")


def ring_gather(piece, name):
    count = lax.axis_size(name)
    here = lax.axis_index(name)
    ahead = [(i, (i + 1) % count) for i in range(count)]
    behind = [(i, (i - 1) % count) for i in range(count)]
    parts = [piece]
    from_left = piece
    from_right = piece
    for step in range(1, count // 2 + 1):
        from_left = lax.ppermute(from_left, name, ahead)
        parts.append(from_left)
        if step < count - step:
            from_right = lax.ppermute(from_right, name, behind)
            parts.append(from_right)
    order = [0] * count
    order[0] = 0
    k = 1
    for step in range(1, count // 2 + 1):
        order[(count - step) % count] = k
        k += 1
        if step < count - step:
            order[step] = k
            k += 1
    stacked = jnp.stack([parts[order[j]] for j in range(count)])
    gathered = jnp.roll(stacked, here, axis=0)
    return gathered.reshape((count * piece.shape[0],) + piece.shape[1:])


def staged_scatter(part, block_rows):
    sizes = tuple(lax.axis_size(name) for name in DP)
    features = part.shape[1]
    held = part.reshape(sizes + (block_rows, features))
    held = jnp.transpose(held, (2, 0, 1, 3, 4))
    total = None
    for name in (DP[2], DP[0], DP[1]):
        arrived = lax.all_to_all(held, name, 0, 0, tiled=True)
        total = jnp.sum(arrived.astype(jnp.float32), axis=0)
        held = total.astype(part.dtype)
    return total.reshape(block_rows, features)


def core_split_sum(part):
    core, chips = MP[1], MP[0]
    upper = lax.axis_index(core) != 0
    swap = [(0, 1), (1, 0)]
    low, high = jnp.split(part, 2, axis=0)
    got = lax.ppermute(jnp.where(upper, low, high), core, swap)
    half = (jnp.where(upper, high, low).astype(jnp.float32) + got.astype(jnp.float32)).astype(part.dtype)
    half = lax.psum(half, chips)
    other = lax.ppermute(half, core, swap)
    return jnp.where(
        upper, jnp.concatenate([other, half], axis=0), jnp.concatenate([half, other], axis=0)
    )


def body(
    store_rows, source_shard, source_row, state_len, visits, gain, w_gate, w_up, w_down, upstream
):
    f32, bf16 = jnp.float32, jnp.bfloat16
    count_dp = 1
    for name in DP:
        count_dp *= lax.axis_size(name)
    index_dp = lax.axis_index(DP)
    total_rows = source_shard.shape[0]
    block_rows = total_rows // count_dp
    pair_cap = max(block_rows // 8, 1)
    store_dev = store_rows.shape[0]
    hidden_dev = w_gate.shape[1]

    shard = source_shard.reshape(count_dp, block_rows)
    srow = source_row.reshape(count_dp, block_rows)
    same = shard[:, :, None] == shard[:, None, :]
    t_ids = jnp.arange(block_rows, dtype=jnp.int32)
    earlier = t_ids[None, :] < t_ids[:, None]
    rank = jnp.sum((same & earlier[None]).astype(jnp.int32), axis=2)

    owned = shard == index_dp
    slots = jnp.arange(pair_cap, dtype=jnp.int32)
    hit = owned[:, :, None] & (rank[:, :, None] == slots[None, None, :])
    slot_row = jnp.sum(jnp.where(hit, srow[:, :, None] + 1, 0), axis=1) - 1
    pick_out = (
        slot_row.reshape(count_dp * pair_cap)[:, None]
        == jnp.arange(store_dev, dtype=jnp.int32)[None, :]
    ).astype(bf16)
    outgoing = jnp.dot(pick_out, store_rows, preferred_element_type=f32).astype(bf16)
    received = lax.all_to_all(outgoing, DP, 0, 0, tiled=True)

    my_shard = lax.dynamic_index_in_dim(shard, index_dp, 0, keepdims=False)
    my_rank = lax.dynamic_index_in_dim(rank, index_dp, 0, keepdims=False)
    pick_in = (
        (my_shard * pair_cap + my_rank)[:, None]
        == jnp.arange(count_dp * pair_cap, dtype=jnp.int32)[None, :]
    ).astype(bf16)
    own_rows = jnp.dot(pick_in, received, preferred_element_type=f32).astype(bf16)

    train_rows = own_rows
    for name in reversed(DP):
        train_rows = ring_gather(train_rows, name)

    row_ids = jnp.arange(total_rows, dtype=jnp.int32)
    ends = jnp.cumsum(state_len)
    starts = ends - state_len
    member = ((row_ids[:, None] >= starts[None, :]) & (row_ids[:, None] < ends[None, :])).astype(
        f32
    )
    importance = jnp.log1p(visits.astype(f32))
    per_state = total_rows * importance / (state_len.astype(f32) * jnp.sum(importance))
    row_weight = jnp.sum(member * per_state[None, :], axis=1)
    out_grad = (upstream.astype(f32) * row_weight[:, None]).astype(bf16)
    hidden_term = lax.dot_general(
        out_grad, w_down, (((1,), (1,)), ((), ())), preferred_element_type=f32
    ).astype(bf16)
    hidden_sum = lax.psum(hidden_term, MP)
    hidden_sum, train_rows = lax.optimization_barrier((hidden_sum, train_rows))
    grad_hidden = hidden_sum.astype(f32)

    rows_float = train_rows.astype(f32)
    squares = jnp.sum(rows_float * rows_float, axis=1)
    scaled = (rows_float * gain.astype(f32)[None, :]).astype(bf16)
    gate_term = jnp.dot(scaled, w_gate, preferred_element_type=f32)
    up_term = jnp.dot(scaled, w_up, preferred_element_type=f32)
    packed = jnp.concatenate([gate_term, up_term, squares[:, None]], axis=1).astype(bf16)
    total = core_split_sum(packed).astype(f32)
    gate_total = total[:, :hidden_dev]
    up_total = total[:, hidden_dev : 2 * hidden_dev]
    square_total = total[:, 2 * hidden_dev]
    inverse = lax.rsqrt(square_total / D + epsilon)
    gate_all = inverse[:, None] * gate_total
    up_all = inverse[:, None] * up_total
    hidden_all = (jax.nn.silu(gate_all) * up_all).astype(bf16)

    down_part = jnp.dot(hidden_all, w_down, preferred_element_type=f32).astype(bf16)
    down_block = staged_scatter(down_part, block_rows)
    layer_out = (own_rows.astype(f32) + down_block).astype(bf16)

    grad_down = lax.dot_general(
        hidden_all, out_grad, (((0,), (0,)), ((), ())), preferred_element_type=f32
    ).astype(bf16)
    sigmoid_gate = jax.nn.sigmoid(gate_all)
    gate_delta = (
        inverse[:, None]
        * grad_hidden
        * up_all
        * sigmoid_gate
        * (1.0 + gate_all * (1.0 - sigmoid_gate))
    ).astype(bf16)
    up_delta = (inverse[:, None] * grad_hidden * gate_all * sigmoid_gate).astype(bf16)
    grad_gate = lax.dot_general(
        scaled, gate_delta, (((0,), (0,)), ((), ())), preferred_element_type=f32
    ).astype(bf16)
    grad_up = lax.dot_general(
        scaled, up_delta, (((0,), (0,)), ((), ())), preferred_element_type=f32
    ).astype(bf16)
    return (layer_out, grad_gate, grad_up, grad_down)


def solution(mesh):
    sizes = dict(zip(mesh.axis_names, mesh.devices.shape))
    count_mp = sizes["mp"]
    count_dp = sizes["dp"]
    zh = 2
    y = 4
    x = count_dp // (zh * y)
    c = 2
    zl = count_mp // c
    view = Mesh(mesh.devices.reshape(x, zh, y, zl, c), DP + MP)
    in_specs = (
        P(DP, MP),
        P(),
        P(),
        P(),
        P(),
        P(MP),
        P(MP, DP),
        P(MP, DP),
        P(DP, MP),
        P(None, MP),
    )
    out_specs = (P(DP, MP), P(MP, DP), P(MP, DP), P(DP, MP))
    return jax.shard_map(body, mesh=view, in_specs=in_specs, out_specs=out_specs, check_vma=False)
```

```python
import jax
import jax.numpy as jnp
from jax import lax
from jax.sharding import Mesh
from jax.sharding import PartitionSpec as P


D = 8192

epsilon = 1e-05

DP = ("x", "zh", "y")
MP = ("zl", "c")


def ring_gather(piece, name):
    count = lax.axis_size(name)
    here = lax.axis_index(name)
    ahead = [(i, (i + 1) % count) for i in range(count)]
    behind = [(i, (i - 1) % count) for i in range(count)]
    parts = [piece]
    from_left = piece
    from_right = piece
    for step in range(1, count // 2 + 1):
        from_left = lax.ppermute(from_left, name, ahead)
        parts.append(from_left)
        if step < count - step:
            from_right = lax.ppermute(from_right, name, behind)
            parts.append(from_right)
    order = [0] * count
    order[0] = 0
    k = 1
    for step in range(1, count // 2 + 1):
        order[(count - step) % count] = k
        k += 1
        if step < count - step:
            order[step] = k
            k += 1
    stacked = jnp.stack([parts[order[j]] for j in range(count)])
    gathered = jnp.roll(stacked, here, axis=0)
    return gathered.reshape((count * piece.shape[0],) + piece.shape[1:])


def staged_scatter(part, block_rows):
    sizes = tuple(lax.axis_size(name) for name in DP)
    features = part.shape[1]
    held = part.reshape(sizes + (block_rows, features))
    held = jnp.transpose(held, (2, 0, 1, 3, 4))
    total = None
    for name in (DP[2], DP[0], DP[1]):
        arrived = lax.all_to_all(held, name, 0, 0, tiled=True)
        total = jnp.sum(arrived.astype(jnp.float32), axis=0)
        held = total.astype(part.dtype)
    return total.reshape(block_rows, features)


def core_split_sum(part):
    core, chips = MP[1], MP[0]
    here = lax.axis_index(core)
    swap = [(0, 1), (1, 0)]
    rows = part.shape[0] // 2
    got = lax.ppermute(lax.dynamic_slice_in_dim(part, (1 - here) * rows, rows, 0), core, swap)
    keep = lax.dynamic_slice_in_dim(part, here * rows, rows, 0)
    half = (keep.astype(jnp.float32) + got.astype(jnp.float32)).astype(part.dtype)
    half = lax.psum(half, chips)
    other = lax.ppermute(half, core, swap)
    whole = lax.dynamic_update_slice_in_dim(jnp.zeros_like(part), half, here * rows, 0)
    return lax.dynamic_update_slice_in_dim(whole, other, (1 - here) * rows, 0)


def body(
    store_rows, source_shard, source_row, state_len, visits, gain, w_gate, w_up, w_down, upstream
):
    f32, bf16 = jnp.float32, jnp.bfloat16
    count_dp = 1
    for name in DP:
        count_dp *= lax.axis_size(name)
    index_dp = lax.axis_index(DP)
    total_rows = source_shard.shape[0]
    block_rows = total_rows // count_dp
    pair_cap = max(block_rows // 8, 1)
    store_dev = store_rows.shape[0]
    hidden_dev = w_gate.shape[1]

    shard = source_shard.reshape(count_dp, block_rows)
    srow = source_row.reshape(count_dp, block_rows)
    same = shard[:, :, None] == shard[:, None, :]
    t_ids = jnp.arange(block_rows, dtype=jnp.int32)
    earlier = t_ids[None, :] < t_ids[:, None]
    rank = jnp.sum((same & earlier[None]).astype(jnp.int32), axis=2)

    owned = shard == index_dp
    slots = jnp.arange(pair_cap, dtype=jnp.int32)
    hit = owned[:, :, None] & (rank[:, :, None] == slots[None, None, :])
    slot_row = jnp.sum(jnp.where(hit, srow[:, :, None] + 1, 0), axis=1) - 1
    pick_out = (
        slot_row.reshape(count_dp * pair_cap)[:, None]
        == jnp.arange(store_dev, dtype=jnp.int32)[None, :]
    ).astype(bf16)
    outgoing = jnp.dot(pick_out, store_rows, preferred_element_type=f32).astype(bf16)
    received = lax.all_to_all(outgoing, DP, 0, 0, tiled=True)

    my_shard = lax.dynamic_index_in_dim(shard, index_dp, 0, keepdims=False)
    my_rank = lax.dynamic_index_in_dim(rank, index_dp, 0, keepdims=False)
    pick_in = (
        (my_shard * pair_cap + my_rank)[:, None]
        == jnp.arange(count_dp * pair_cap, dtype=jnp.int32)[None, :]
    ).astype(bf16)
    own_rows = jnp.dot(pick_in, received, preferred_element_type=f32).astype(bf16)

    train_rows = own_rows
    for name in reversed(DP):
        train_rows = ring_gather(train_rows, name)

    row_ids = jnp.arange(total_rows, dtype=jnp.int32)
    ends = jnp.cumsum(state_len)
    starts = ends - state_len
    member = ((row_ids[:, None] >= starts[None, :]) & (row_ids[:, None] < ends[None, :])).astype(
        f32
    )
    importance = jnp.log1p(visits.astype(f32))
    per_state = total_rows * importance / (state_len.astype(f32) * jnp.sum(importance))
    row_weight = jnp.sum(member * per_state[None, :], axis=1)
    out_grad = (upstream.astype(f32) * row_weight[:, None]).astype(bf16)
    hidden_term = lax.dot_general(
        out_grad, w_down, (((1,), (1,)), ((), ())), preferred_element_type=f32
    ).astype(bf16)
    hidden_sum = lax.psum(hidden_term, MP)
    hidden_sum, train_rows = lax.optimization_barrier((hidden_sum, train_rows))
    grad_hidden = hidden_sum.astype(f32)

    rows_float = train_rows.astype(f32)
    squares = jnp.sum(rows_float * rows_float, axis=1)
    scaled = (rows_float * gain.astype(f32)[None, :]).astype(bf16)
    gate_term = jnp.dot(scaled, w_gate, preferred_element_type=f32)
    up_term = jnp.dot(scaled, w_up, preferred_element_type=f32)
    packed = jnp.concatenate([gate_term, up_term, squares[:, None]], axis=1).astype(bf16)
    total = core_split_sum(packed).astype(f32)
    gate_total = total[:, :hidden_dev]
    up_total = total[:, hidden_dev : 2 * hidden_dev]
    square_total = total[:, 2 * hidden_dev]
    inverse = lax.rsqrt(square_total / D + epsilon)
    gate_all = inverse[:, None] * gate_total
    up_all = inverse[:, None] * up_total
    hidden_all = (jax.nn.silu(gate_all) * up_all).astype(bf16)

    down_part = jnp.dot(hidden_all, w_down, preferred_element_type=f32).astype(bf16)
    down_block = staged_scatter(down_part, block_rows)
    layer_out = (own_rows.astype(f32) + down_block).astype(bf16)

    grad_down = lax.dot_general(
        hidden_all, out_grad, (((0,), (0,)), ((), ())), preferred_element_type=f32
    ).astype(bf16)
    sigmoid_gate = jax.nn.sigmoid(gate_all)
    gate_delta = (
        inverse[:, None]
        * grad_hidden
        * up_all
        * sigmoid_gate
        * (1.0 + gate_all * (1.0 - sigmoid_gate))
    ).astype(bf16)
    up_delta = (inverse[:, None] * grad_hidden * gate_all * sigmoid_gate).astype(bf16)
    grad_gate = lax.dot_general(
        scaled, gate_delta, (((0,), (0,)), ((), ())), preferred_element_type=f32
    ).astype(bf16)
    grad_up = lax.dot_general(
        scaled, up_delta, (((0,), (0,)), ((), ())), preferred_element_type=f32
    ).astype(bf16)
    return (layer_out, grad_gate, grad_up, grad_down)


def solution(mesh):
    sizes = dict(zip(mesh.axis_names, mesh.devices.shape))
    count_mp = sizes["mp"]
    count_dp = sizes["dp"]
    zh = 2
    y = 4
    x = count_dp // (zh * y)
    c = 2
    zl = count_mp // c
    view = Mesh(mesh.devices.reshape(x, zh, y, zl, c), DP + MP)
    in_specs = (
        P(DP, MP),
        P(),
        P(),
        P(),
        P(),
        P(MP),
        P(MP, DP),
        P(MP, DP),
        P(DP, MP),
        P(None, MP),
    )
    out_specs = (P(DP, MP), P(MP, DP), P(MP, DP), P(DP, MP))
    return jax.shard_map(body, mesh=view, in_specs=in_specs, out_specs=out_specs, check_vma=False)
```
